128 devices in a mesh: wide: 16 (over z, y), narrow: 8 (over x, core).
Axes of the slice: x: 4, y: 4, z: 4, core: 2. Of those that a mesh axis runs over, the one named last changes fastest.
Arguments:
- matrix_panel: float32 [8, 16777216], P(None, ('wide', 'narrow')), may hold values from -6 to 6
- sign_bits: int32 [16777216], P(('wide', 'narrow')), may hold values from 0 to 1
Outputs:
- mixed_panel: float32 [8, 16777216], P(None, ('wide', 'narrow'))
The draws below stay inside these ranges and needn't reach their ends.
All inputs are finite; a program needn't handle non-finite values.
Results may differ from the reference program's by a relative error of at most 0.000086.
Values sent between devices are 32-bit elements; how exact they have to be, the bound alone decides.
No kernel may reach another device: no remote copies, remote signals or barrier semaphores. Data moves between devices by JAX's collectives and lax.ppermute only.
A program may use at most 64 MiB of HBM per device.

```python
import math
import jax
import jax.numpy as jnp

COLS = 8
LENGTH = 16777216


def set_ends(entries, key, least, largest):
    shape = entries.shape
    spot = [jax.random.randint(jax.random.fold_in(key, axis), (), 0, shape[axis]) for axis in range(len(shape))]
    entries = entries.at[tuple(spot)].set(least)
    longest = shape.index(max(shape))
    spot[longest] = (spot[longest] + 1) % shape[longest]
    return entries.at[tuple(spot)].set(largest)


def level_of(stream_key, shape, pieces, smallest, largest):
    def one(position, parts):
        steps = jax.random.uniform(jax.random.fold_in(jax.random.fold_in(stream_key, 6), position), (parts,), jnp.float32, smallest / len(pieces), largest / len(pieces))
        return jnp.repeat(jnp.exp(steps), shape[position] // parts).reshape((-1,) + (1,) * (len(shape) - position - 1))

    gain = one(*pieces[0])
    for cut in pieces[1:]:
        gain = gain * one(*cut)
    return gain


def scatter_about(key, shape, deviation, limit, split=(), kind=jnp.bfloat16):
    loudness = level_of(key, shape, split, -0.22, 0.18) if split else 1.0
    drawn = jax.random.normal(key, shape, jnp.float32) * deviation * loudness
    return jnp.minimum(jnp.maximum(drawn, -limit), limit).astype(kind)


def setup_inputs(seed: int = 0) -> dict:
    key_list = jax.random.split(jax.random.key(seed), 3)
    matrix_panel = scatter_about(key_list[0], (COLS, LENGTH), 1.0, 6.0, ((1, 128),), jnp.float32)
    sign_bits = set_ends(jax.random.randint(key_list[1], (LENGTH,), 0, 2), jax.random.fold_in(key_list[1], 1), 0, 1).astype(jnp.int32)
    return dict(matrix_panel=matrix_panel, sign_bits=sign_bits)


def reference(matrix_panel, sign_bits):
    signed = matrix_panel * (2 * sign_bits - 1).astype(jnp.float32)[None, :]
    columns, length = signed.shape
    levels = int(length).bit_length() - 1
    current = signed
    half = 1
    for level in range(levels):
        shaped = current.reshape(columns, length // (2 * half), 2, half)
        first = shaped[:, :, 0, :]
        second = shaped[:, :, 1, :]
        current = jnp.stack([first + second, first - second], axis=2).reshape(columns, length)
        half = half * 2
    return current * jnp.float32(1.0 / math.sqrt(length))
```

```python
import math

import jax
import jax.numpy as jnp
from jax import lax
from jax.sharding import PartitionSpec as P


def hadamard_table(order):
    index = jnp.arange(order, dtype=jnp.int32)
    common = jnp.bitwise_and(index[:, None], index[None, :])
    parity = jnp.zeros((order, order), jnp.int32)
    for level in range(max(order.bit_length() - 1, 0)):
        parity = parity + jnp.bitwise_and(jnp.right_shift(common, level), 1)
    return (1 - 2 * jnp.bitwise_and(parity, 1)).astype(jnp.float32)


def local_transform(values):
    columns, length = values.shape
    factors = []
    remain = length
    while remain > 1:
        factor = min(128, remain)
        factors.insert(0, factor)
        remain = remain // factor
    before = 1
    for factor in factors:
        after = length // (before * factor)
        table = hadamard_table(factor)
        if after > 1:
            shaped = values.reshape(columns, before, factor, after)
            shaped = jnp.einsum("cafb,gf->cagb", shaped, table, precision=lax.Precision.HIGHEST)
        else:
            shaped = values.reshape(columns, before, factor)
            shaped = jnp.einsum("caf,gf->cag", shaped, table, precision=lax.Precision.HIGHEST)
        values = shaped.reshape(columns, length)
        before = before * factor
    return values


AXES = ("wide", "narrow")


def body(matrix_panel, sign_bits):
    signed = matrix_panel * (2 * sign_bits - 1).astype(jnp.float32)[None, :]
    current = local_transform(signed)
    columns, length = current.shape
    devices = lax.axis_size("wide") * lax.axis_size("narrow")
    blocks = current.reshape(columns, devices, length // devices)
    gathered = lax.all_to_all(blocks, AXES, split_axis=1, concat_axis=1, tiled=True)
    mixed = jnp.einsum(
        "csr,vs->cvr", gathered, hadamard_table(devices), precision=lax.Precision.HIGHEST
    )
    current = lax.all_to_all(mixed, AXES, split_axis=1, concat_axis=1, tiled=True)
    scale = jnp.float32(1.0 / math.sqrt(length * devices))
    return current.reshape(columns, length) * scale


def solution(mesh):
    in_specs = (P(None, AXES), P(AXES))
    out_specs = P(None, AXES)
    return jax.shard_map(body, mesh=mesh, in_specs=in_specs, out_specs=out_specs, check_vma=False)
```

```python
import math

import jax
import jax.numpy as jnp
from jax import lax
from jax.experimental import pallas as pl
from jax.experimental.pallas import tpu as pltpu
from jax.sharding import PartitionSpec as P

AXES = ("wide", "narrow")
LANES = 128


def hadamard_table(order):
    index = jnp.arange(order, dtype=jnp.int32)
    common = jnp.bitwise_and(index[:, None], index[None, :])
    parity = jnp.zeros((order, order), jnp.int32)
    for level in range(max(order.bit_length() - 1, 0)):
        parity = parity + jnp.bitwise_and(jnp.right_shift(common, level), 1)
    return (1 - 2 * jnp.bitwise_and(parity, 1)).astype(jnp.float32)


def butterfly(vals):
    n = len(vals)
    half = 1
    while half < n:
        out = list(vals)
        for i in range(n):
            if not i & half:
                a, b = vals[i], vals[i | half]
                out[i] = a + b
                out[i | half] = a - b
        vals = out
        half *= 2
    return vals


def radix_pass(src, dst, rows, low, bits, pre=None, post=None):
    span = 1 << bits
    stride = 1 << low

    def step(g, carry):
        base = (g // stride) * (stride * span) + g % stride
        vals = [src[base + j * stride] for j in range(span)]
        if pre is not None:
            vals = pre(vals, base, stride)
        vals = butterfly(vals)
        if post is not None:
            vals = [post(v) for v in vals]
        for j in range(span):
            dst[base + j * stride] = vals[j]
        return carry

    lax.fori_loop(0, rows // span, step, 0)


def pre_kernel(x_ref, s_ref, h_ref, o_ref):
    rows = x_ref.shape[0]
    table = h_ref[...]

    def signed_lanes(vals, base, stride):
        out = []
        for j, v in enumerate(vals):
            sign = s_ref[pl.ds(base + j * stride, 1), :].astype(jnp.float32) * 2.0 - 1.0
            out.append(v * sign)
        block = jnp.concatenate(out, axis=0)
        mixed = jnp.dot(block, table, precision=lax.Precision.HIGHEST,
                        preferred_element_type=jnp.float32)
        cols = vals[0].shape[0]
        return [mixed[j * cols:(j + 1) * cols] for j in range(len(vals))]

    radix_pass(x_ref, o_ref, rows, 3, 4, pre=signed_lanes)
    radix_pass(o_ref, o_ref, rows, 7, 3)


def mid_kernel(x_ref, o_ref, *, scale):
    rows = x_ref.shape[0]
    radix_pass(x_ref, o_ref, rows, 0, 4)
    radix_pass(o_ref, o_ref, rows, 4, 3)
    radix_pass(o_ref, o_ref, rows, 7, 3, post=lambda v: v * scale)


def vmem_call(kernel, out_shape, n_in):
    return pl.pallas_call(
        kernel,
        out_shape=out_shape,
        in_specs=[pl.BlockSpec(memory_space=pltpu.VMEM)] * n_in,
        out_specs=pl.BlockSpec(memory_space=pltpu.VMEM),
        compiler_params=pltpu.CompilerParams(vmem_limit_bytes=48 * 1024 * 1024),
    )


def body(matrix_panel, sign_bits):
    columns, length = matrix_panel.shape
    devices = lax.axis_size("wide") * lax.axis_size("narrow")
    rows = length // LANES
    x = matrix_panel.reshape(columns, rows, LANES).transpose(1, 0, 2)
    signs = sign_bits.reshape(rows, LANES)
    shape = jax.ShapeDtypeStruct((rows, columns, LANES), jnp.float32)
    y = vmem_call(pre_kernel, shape, 3)(x, signs, hadamard_table(LANES))
    blocks = y.reshape(devices, rows // devices, columns, LANES)
    gathered = lax.all_to_all(blocks, AXES, 0, 0, tiled=True).reshape(rows, columns, LANES)
    scale = 1.0 / math.sqrt(length * devices)
    mixed = vmem_call(lambda a, b: mid_kernel(a, b, scale=scale), shape, 1)(gathered)
    back = lax.all_to_all(mixed.reshape(blocks.shape), AXES, 0, 0, tiled=True)
    return back.reshape(rows, columns, LANES).transpose(1, 0, 2).reshape(columns, length)


def solution(mesh):
    in_specs = (P(None, AXES), P(AXES))
    out_specs = P(None, AXES)
    return jax.shard_map(body, mesh=mesh, in_specs=in_specs, out_specs=out_specs, check_vma=False)
```

```python
import functools
import math

import jax
import jax.numpy as jnp
from jax import lax
from jax.experimental import pallas as pl
from jax.experimental.pallas import tpu as pltpu
from jax.sharding import PartitionSpec as P

AXES = ("wide", "narrow")
LANES = 128


def hadamard_table(order):
    index = jnp.arange(order, dtype=jnp.int32)
    common = jnp.bitwise_and(index[:, None], index[None, :])
    parity = jnp.zeros((order, order), jnp.int32)
    for level in range(max(order.bit_length() - 1, 0)):
        parity = parity + jnp.bitwise_and(jnp.right_shift(common, level), 1)
    return (1 - 2 * jnp.bitwise_and(parity, 1)).astype(jnp.float32)


def butterfly(vals):
    n = len(vals)
    half = 1
    while half < n:
        out = list(vals)
        for i in range(n):
            if not i & half:
                a, b = vals[i], vals[i | half]
                out[i] = a + b
                out[i | half] = a - b
        vals = out
        half *= 2
    return vals


def radix_pass(src, dst, rows, low, bits, pre=None, post=None):
    span = 1 << bits
    stride = 1 << low

    def step(g, carry):
        base = (g // stride) * (stride * span) + g % stride
        vals = [src[base + j * stride] for j in range(span)]
        if pre is not None:
            vals = pre(vals, base, stride)
        vals = butterfly(vals)
        if post is not None:
            vals = [post(v) for v in vals]
        for j in range(span):
            dst[base + j * stride] = vals[j]
        return carry

    lax.fori_loop(0, rows // span, step, 0)


CHUNKS = 8


def split_rows(block):
    high = block.astype(jnp.bfloat16)
    rest = (block - high.astype(jnp.float32)).astype(jnp.bfloat16)
    return jnp.concatenate([high, rest], axis=0)


def chunked_kernel(x_hbm, *refs, inner, outer, signed):
    if signed:
        s_ref, h_ref, o_ref, buf, sems = refs
    else:
        o_ref, buf, sems = refs
    rows = o_ref.shape[0]
    size = rows // CHUNKS
    copies = [
        pltpu.make_async_copy(x_hbm.at[pl.ds(i * size, size)], buf.at[pl.ds(i * size, size)], sems.at[i])
        for i in range(CHUNKS)
    ]
    for copy in copies:
        copy.start()

    def signed_lanes(vals, base, stride):
        table = h_ref[...]
        cols = vals[0].shape[0]
        out = []
        for j, v in enumerate(vals):
            sign = s_ref[pl.ds(base + j * stride, 1), :].astype(jnp.float32) * 2.0 - 1.0
            out.append(v * sign)
        block = jnp.concatenate(out, axis=0)
        both = jnp.dot(split_rows(block), table, preferred_element_type=jnp.float32)
        count = block.shape[0]
        mixed = both[:count] + both[count:]
        return [mixed[j * cols:(j + 1) * cols] for j in range(len(vals))]

    for i, copy in enumerate(copies):
        copy.wait()
        src = buf.at[pl.ds(i * size, size)]
        dst = o_ref.at[pl.ds(i * size, size)]
        for n, (low, bits) in enumerate(inner):
            pre = signed_lanes if (signed and n == 0) else None
            if pre is not None:
                offset = i * size
                pre = (lambda f, o: (lambda vals, base, stride: f(vals, base + o, stride)))(signed_lanes, offset)
            radix_pass(src if n == 0 else dst, dst, size, low, bits, pre=pre)
    for n, (low, bits, post) in enumerate(outer):
        radix_pass(o_ref, o_ref, rows, low, bits, post=post)


def chunked_call(out_shape, *, inner, outer, signed):
    n_vmem = 2 if signed else 0
    kernel = functools.partial(chunked_kernel, inner=inner, outer=outer, signed=signed)
    return pl.pallas_call(
        kernel,
        out_shape=out_shape,
        in_specs=[pl.BlockSpec(memory_space=pl.ANY)] + [pl.BlockSpec(memory_space=pltpu.VMEM)] * n_vmem,
        out_specs=pl.BlockSpec(memory_space=pltpu.VMEM),
        scratch_shapes=[pltpu.VMEM(out_shape.shape, jnp.float32), pltpu.SemaphoreType.DMA((CHUNKS,))],
        compiler_params=pltpu.CompilerParams(vmem_limit_bytes=48 * 1024 * 1024),
    )


def body(matrix_panel, sign_bits):
    columns, length = matrix_panel.shape
    devices = lax.axis_size("wide") * lax.axis_size("narrow")
    rows = length // LANES
    x = matrix_panel.reshape(columns, rows, LANES).transpose(1, 0, 2)
    signs = sign_bits.reshape(rows, LANES)
    shape = jax.ShapeDtypeStruct((rows, columns, LANES), jnp.float32)
    table = hadamard_table(LANES).astype(jnp.bfloat16)
    y = chunked_call(shape, inner=((3, 4),), outer=((7, 3, None),), signed=True)(x, signs, table)
    blocks = y.reshape(devices, rows // devices, columns, LANES)
    gathered = lax.all_to_all(blocks, AXES, 0, 0, tiled=True).reshape(rows, columns, LANES)
    scale = 1.0 / math.sqrt(length * devices)
    mid = chunked_call(shape, inner=((0, 4), (4, 3)), outer=((7, 3, lambda v: v * scale),), signed=False)
    mixed = mid(gathered)
    back = lax.all_to_all(mixed.reshape(blocks.shape), AXES, 0, 0, tiled=True)
    return back.reshape(rows, columns, LANES).transpose(1, 0, 2).reshape(columns, length)


def solution(mesh):
    in_specs = (P(None, AXES), P(AXES))
    out_specs = P(None, AXES)
    return jax.shard_map(body, mesh=mesh, in_specs=in_specs, out_specs=out_specs, check_vma=False)
```

```python
import functools
import math

import jax
import jax.numpy as jnp
from jax import lax
from jax.experimental import pallas as pl
from jax.experimental.pallas import tpu as pltpu
from jax.sharding import PartitionSpec as P

AXES = ("wide", "narrow")
LANES = 128


def hadamard_table(order):
    index = jnp.arange(order, dtype=jnp.int32)
    common = jnp.bitwise_and(index[:, None], index[None, :])
    parity = jnp.zeros((order, order), jnp.int32)
    for level in range(max(order.bit_length() - 1, 0)):
        parity = parity + jnp.bitwise_and(jnp.right_shift(common, level), 1)
    return (1 - 2 * jnp.bitwise_and(parity, 1)).astype(jnp.float32)


def butterfly(vals):
    n = len(vals)
    half = 1
    while half < n:
        out = list(vals)
        for i in range(n):
            if not i & half:
                a, b = vals[i], vals[i | half]
                out[i] = a + b
                out[i | half] = a - b
        vals = out
        half *= 2
    return vals


def radix_pass(src, dst, rows, low, bits, post=None):
    span = 1 << bits
    stride = 1 << low
    for g in range(rows // span):
        base = (g // stride) * (stride * span) + g % stride
        vals = butterfly([src[base + j * stride] for j in range(span)])
        for j in range(span):
            dst[base + j * stride] = vals[j] if post is None else post(vals[j])


CHUNKS = 8


def split_rows(block):
    high = block.astype(jnp.bfloat16)
    rest = (block - high.astype(jnp.float32)).astype(jnp.bfloat16)
    return jnp.concatenate([high, rest], axis=0)


def chunked_kernel(x_hbm, *refs, inner, outer, signed):
    if signed:
        s_ref, h_ref, o_ref, buf, sems = refs
    else:
        o_ref, buf, sems = refs
    rows = o_ref.shape[0]
    size = rows // CHUNKS
    copies = [
        pltpu.make_async_copy(x_hbm.at[pl.ds(i * size, size)], buf.at[pl.ds(i * size, size)], sems.at[i])
        for i in range(CHUNKS)
    ]
    for copy in copies:
        copy.start()

    for i, copy in enumerate(copies):
        copy.wait()
        rows_here = pl.ds(i * size, size)
        dst = o_ref.at[rows_here]
        if signed:
            block = buf[rows_here]
            sign = s_ref[rows_here, :].astype(jnp.float32) * 2.0 - 1.0
            block = (block * sign[:, None, :]).reshape(size * block.shape[1], block.shape[2])
            both = jnp.dot(split_rows(block), h_ref[...], preferred_element_type=jnp.float32)
            count = block.shape[0]
            dst[...] = (both[:count] + both[count:]).reshape(dst.shape)
            first = dst
        else:
            first = buf.at[rows_here]
        for n, (low, bits) in enumerate(inner):
            radix_pass(first if n == 0 else dst, dst, size, low, bits)
    for n, (low, bits, post) in enumerate(outer):
        radix_pass(o_ref, o_ref, rows, low, bits, post=post)


def chunked_call(out_shape, *, inner, outer, signed):
    n_vmem = 2 if signed else 0
    kernel = functools.partial(chunked_kernel, inner=inner, outer=outer, signed=signed)
    return pl.pallas_call(
        kernel,
        out_shape=out_shape,
        in_specs=[pl.BlockSpec(memory_space=pl.ANY)] + [pl.BlockSpec(memory_space=pltpu.VMEM)] * n_vmem,
        out_specs=pl.BlockSpec(memory_space=pltpu.VMEM),
        scratch_shapes=[pltpu.VMEM(out_shape.shape, jnp.float32), pltpu.SemaphoreType.DMA((CHUNKS,))],
        compiler_params=pltpu.CompilerParams(vmem_limit_bytes=48 * 1024 * 1024),
    )


def body(matrix_panel, sign_bits):
    columns, length = matrix_panel.shape
    devices = lax.axis_size("wide") * lax.axis_size("narrow")
    rows = length // LANES
    x = matrix_panel.reshape(columns, rows, LANES).transpose(1, 0, 2)
    signs = sign_bits.reshape(rows, LANES)
    shape = jax.ShapeDtypeStruct((rows, columns, LANES), jnp.float32)
    table = hadamard_table(LANES).astype(jnp.bfloat16)
    y = chunked_call(shape, inner=((3, 4),), outer=((7, 3, None),), signed=True)(x, signs, table)
    blocks = y.reshape(devices, rows // devices, columns, LANES)
    gathered = lax.all_to_all(blocks, AXES, 0, 0, tiled=True).reshape(rows, columns, LANES)
    scale = 1.0 / math.sqrt(length * devices)
    mid = chunked_call(shape, inner=((0, 4), (4, 3)), outer=((7, 3, lambda v: v * scale),), signed=False)
    mixed = mid(gathered)
    back = lax.all_to_all(mixed.reshape(blocks.shape), AXES, 0, 0, tiled=True)
    return back.reshape(rows, columns, LANES).transpose(1, 0, 2).reshape(columns, length)


def solution(mesh):
    in_specs = (P(None, AXES), P(AXES))
    out_specs = P(None, AXES)
    return jax.shard_map(body, mesh=mesh, in_specs=in_specs, out_specs=out_specs, check_vma=False)
```

```python
import functools
import math

import jax
import jax.numpy as jnp
from jax import lax
from jax.experimental import pallas as pl
from jax.experimental.pallas import tpu as pltpu
from jax.sharding import PartitionSpec as P

AXES = ("wide", "narrow")
GROUP = ("narrow", "wide")
LANES = 128


def hadamard_table(order):
    index = jnp.arange(order, dtype=jnp.int32)
    common = jnp.bitwise_and(index[:, None], index[None, :])
    parity = jnp.zeros((order, order), jnp.int32)
    for level in range(max(order.bit_length() - 1, 0)):
        parity = parity + jnp.bitwise_and(jnp.right_shift(common, level), 1)
    return (1 - 2 * jnp.bitwise_and(parity, 1)).astype(jnp.float32)


def butterfly(vals):
    n = len(vals)
    half = 1
    while half < n:
        out = list(vals)
        for i in range(n):
            if not i & half:
                a, b = vals[i], vals[i | half]
                out[i] = a + b
                out[i | half] = a - b
        vals = out
        half *= 2
    return vals


def radix_pass(src, dst, rows, low, bits, post=None):
    span = 1 << bits
    stride = 1 << low
    for g in range(rows // span):
        base = (g // stride) * (stride * span) + g % stride
        vals = butterfly([src[base + j * stride] for j in range(span)])
        for j in range(span):
            dst[base + j * stride] = vals[j] if post is None else post(vals[j])


CHUNKS = 8


def split_rows(block):
    high = block.astype(jnp.bfloat16)
    rest = (block - high.astype(jnp.float32)).astype(jnp.bfloat16)
    return jnp.concatenate([high, rest], axis=0)


def chunked_kernel(x_hbm, *refs, inner, outer, signed):
    if signed:
        s_ref, h_ref, o_ref, buf, sems = refs
    else:
        o_ref, buf, sems = refs
    rows = o_ref.shape[0]
    size = rows // CHUNKS
    copies = [
        pltpu.make_async_copy(x_hbm.at[pl.ds(i * size, size)], buf.at[pl.ds(i * size, size)], sems.at[i])
        for i in range(CHUNKS)
    ]
    for copy in copies:
        copy.start()

    for i, copy in enumerate(copies):
        copy.wait()
        rows_here = pl.ds(i * size, size)
        dst = o_ref.at[rows_here]
        if signed:
            block = buf[rows_here]
            sign = s_ref[rows_here, :].astype(jnp.float32) * 2.0 - 1.0
            block = (block * sign[:, None, :]).reshape(size * block.shape[1], block.shape[2])
            both = jnp.dot(split_rows(block), h_ref[...], preferred_element_type=jnp.float32)
            count = block.shape[0]
            dst[...] = (both[:count] + both[count:]).reshape(dst.shape)
            first = dst
        else:
            first = buf.at[rows_here]
        for n, (low, bits) in enumerate(inner):
            radix_pass(first if n == 0 else dst, dst, size, low, bits)
    for n, (low, bits, post) in enumerate(outer):
        radix_pass(o_ref, o_ref, rows, low, bits, post=post)


def chunked_call(out_shape, *, inner, outer, signed):
    n_vmem = 2 if signed else 0
    kernel = functools.partial(chunked_kernel, inner=inner, outer=outer, signed=signed)
    return pl.pallas_call(
        kernel,
        out_shape=out_shape,
        in_specs=[pl.BlockSpec(memory_space=pl.ANY)] + [pl.BlockSpec(memory_space=pltpu.VMEM)] * n_vmem,
        out_specs=pl.BlockSpec(memory_space=pltpu.VMEM),
        scratch_shapes=[pltpu.VMEM(out_shape.shape, jnp.float32), pltpu.SemaphoreType.DMA((CHUNKS,))],
        compiler_params=pltpu.CompilerParams(vmem_limit_bytes=48 * 1024 * 1024),
    )


def body(matrix_panel, sign_bits):
    columns, length = matrix_panel.shape
    devices = lax.axis_size("wide") * lax.axis_size("narrow")
    rows = length // LANES
    x = matrix_panel.reshape(columns, rows, LANES).transpose(1, 0, 2)
    signs = sign_bits.reshape(rows, LANES)
    shape = jax.ShapeDtypeStruct((rows, columns, LANES), jnp.float32)
    table = hadamard_table(LANES).astype(jnp.bfloat16)
    y = chunked_call(shape, inner=((3, 4),), outer=((7, 3, None),), signed=True)(x, signs, table)
    blocks = y.reshape(devices, rows // devices, columns, LANES)
    gathered = lax.all_to_all(blocks, GROUP, 0, 0, tiled=True).reshape(rows, columns, LANES)
    scale = 1.0 / math.sqrt(length * devices)
    mid = chunked_call(shape, inner=((0, 4), (4, 3)), outer=((7, 3, lambda v: v * scale),), signed=False)
    mixed = mid(gathered)
    back = lax.all_to_all(mixed.reshape(blocks.shape), GROUP, 0, 0, tiled=True)
    return back.reshape(rows, columns, LANES).transpose(1, 0, 2).reshape(columns, length)


def solution(mesh):
    in_specs = (P(None, AXES), P(AXES))
    out_specs = P(None, AXES)
    return jax.shard_map(body, mesh=mesh, in_specs=in_specs, out_specs=out_specs, check_vma=False)
```

```python
import functools
import math

import jax
import jax.numpy as jnp
from jax import lax
from jax.experimental import pallas as pl
from jax.experimental.pallas import tpu as pltpu
from jax.sharding import PartitionSpec as P

AXES = ("wide", "narrow")
GROUP = ("narrow", "wide")
LANES = 128


def hadamard_table(order):
    index = jnp.arange(order, dtype=jnp.int32)
    common = jnp.bitwise_and(index[:, None], index[None, :])
    parity = jnp.zeros((order, order), jnp.int32)
    for level in range(max(order.bit_length() - 1, 0)):
        parity = parity + jnp.bitwise_and(jnp.right_shift(common, level), 1)
    return (1 - 2 * jnp.bitwise_and(parity, 1)).astype(jnp.float32)


def butterfly(vals):
    n = len(vals)
    half = 1
    while half < n:
        out = list(vals)
        for i in range(n):
            if not i & half:
                a, b = vals[i], vals[i | half]
                out[i] = a + b
                out[i | half] = a - b
        vals = out
        half *= 2
    return vals


def radix_pass(src, dst, rows, low, bits, post=None):
    span = 1 << bits
    stride = 1 << low
    for g in range(rows // span):
        base = (g // stride) * (stride * span) + g % stride
        vals = butterfly([src[base + j * stride] for j in range(span)])
        for j in range(span):
            dst[base + j * stride] = vals[j] if post is None else post(vals[j])


CHUNKS = 8


def split_rows(block):
    high = block.astype(jnp.bfloat16)
    rest = (block - high.astype(jnp.float32)).astype(jnp.bfloat16)
    return jnp.concatenate([high, rest], axis=0)


def pre_kernel(x_hbm, s_ref, h_ref, o_ref, buf, sems):
    blocks, chunks, cols, lanes = o_ref.shape
    copies = [
        pltpu.make_async_copy(x_hbm.at[:, i], buf.at[i], sems.at[i]) for i in range(chunks)
    ]
    for copy in copies:
        copy.start()
    low = 16
    for i, copy in enumerate(copies):
        copy.wait()
        block = buf[i]
        sign = s_ref[pl.ds(i, blocks, stride=chunks), :].astype(jnp.float32) * 2.0 - 1.0
        block = (block * sign[:, None, :]).reshape(blocks * cols, lanes)
        both = jnp.dot(split_rows(block), h_ref[...], preferred_element_type=jnp.float32)
        count = blocks * cols
        for g in range(blocks // low):
            vals = []
            for j in range(low):
                r = (g * low + j) * cols
                vals.append(both[r:r + cols] + both[count + r:count + r + cols])
            vals = butterfly(vals)
            for j in range(low):
                o_ref[g * low + j, i] = vals[j]
        for j in range(low):
            vals = butterfly([o_ref[g * low + j, i] for g in range(blocks // low)])
            for g in range(blocks // low):
                o_ref[g * low + j, i] = vals[g]


def pre_call(out_shape):
    blocks, chunks, cols, lanes = out_shape.shape
    return pl.pallas_call(
        pre_kernel,
        out_shape=out_shape,
        in_specs=[pl.BlockSpec(memory_space=pl.ANY)] + [pl.BlockSpec(memory_space=pltpu.VMEM)] * 2,
        out_specs=pl.BlockSpec(memory_space=pltpu.VMEM),
        scratch_shapes=[pltpu.VMEM((chunks, blocks, cols, lanes), jnp.float32),
                        pltpu.SemaphoreType.DMA((chunks,))],
        compiler_params=pltpu.CompilerParams(vmem_limit_bytes=48 * 1024 * 1024),
    )


def chunked_kernel(x_hbm, *refs, inner, outer, signed):
    if signed:
        s_ref, h_ref, o_ref, buf, sems = refs
    else:
        o_ref, buf, sems = refs
    rows = o_ref.shape[0]
    size = rows // CHUNKS
    copies = [
        pltpu.make_async_copy(x_hbm.at[pl.ds(i * size, size)], buf.at[pl.ds(i * size, size)], sems.at[i])
        for i in range(CHUNKS)
    ]
    for copy in copies:
        copy.start()

    for i, copy in enumerate(copies):
        copy.wait()
        rows_here = pl.ds(i * size, size)
        dst = o_ref.at[rows_here]
        if signed:
            block = buf[rows_here]
            sign = s_ref[rows_here, :].astype(jnp.float32) * 2.0 - 1.0
            block = (block * sign[:, None, :]).reshape(size * block.shape[1], block.shape[2])
            both = jnp.dot(split_rows(block), h_ref[...], preferred_element_type=jnp.float32)
            count = block.shape[0]
            dst[...] = (both[:count] + both[count:]).reshape(dst.shape)
            first = dst
        else:
            first = buf.at[rows_here]
        for n, (low, bits) in enumerate(inner):
            radix_pass(first if n == 0 else dst, dst, size, low, bits)
    for n, (low, bits, post) in enumerate(outer):
        radix_pass(o_ref, o_ref, rows, low, bits, post=post)


def chunked_call(out_shape, *, inner, outer, signed):
    n_vmem = 2 if signed else 0
    kernel = functools.partial(chunked_kernel, inner=inner, outer=outer, signed=signed)
    return pl.pallas_call(
        kernel,
        out_shape=out_shape,
        in_specs=[pl.BlockSpec(memory_space=pl.ANY)] + [pl.BlockSpec(memory_space=pltpu.VMEM)] * n_vmem,
        out_specs=pl.BlockSpec(memory_space=pltpu.VMEM),
        scratch_shapes=[pltpu.VMEM(out_shape.shape, jnp.float32), pltpu.SemaphoreType.DMA((CHUNKS,))],
        compiler_params=pltpu.CompilerParams(vmem_limit_bytes=48 * 1024 * 1024),
    )


def body(matrix_panel, sign_bits):
    columns, length = matrix_panel.shape
    devices = lax.axis_size("wide") * lax.axis_size("narrow")
    rows = length // LANES
    x = matrix_panel.reshape(columns, rows, LANES).transpose(1, 0, 2)
    signs = sign_bits.reshape(rows, LANES)
    shape = jax.ShapeDtypeStruct((rows, columns, LANES), jnp.float32)
    table = hadamard_table(LANES).astype(jnp.bfloat16)
    block_shape = jax.ShapeDtypeStruct((devices, rows // devices, columns, LANES), jnp.float32)
    blocks = pre_call(block_shape)(x.reshape(block_shape.shape), signs, table)
    gathered = lax.all_to_all(blocks, GROUP, 0, 0, tiled=True).reshape(rows, columns, LANES)
    scale = 1.0 / math.sqrt(length * devices)
    mid = chunked_call(shape, inner=((0, 4), (4, 3)), outer=((7, 3, lambda v: v * scale),), signed=False)
    mixed = mid(gathered)
    back = lax.all_to_all(mixed.reshape(blocks.shape), GROUP, 0, 0, tiled=True)
    return back.reshape(rows, columns, LANES).transpose(1, 0, 2).reshape(columns, length)


def solution(mesh):
    in_specs = (P(None, AXES), P(AXES))
    out_specs = P(None, AXES)
    return jax.shard_map(body, mesh=mesh, in_specs=in_specs, out_specs=out_specs, check_vma=False)
```

```python
import functools
import math

import jax
import jax.numpy as jnp
from jax import lax
from jax.experimental import pallas as pl
from jax.experimental.pallas import tpu as pltpu
from jax.sharding import PartitionSpec as P

AXES = ("wide", "narrow")
GROUP = ("narrow", "wide")
LANES = 128


def hadamard_table(order):
    index = jnp.arange(order, dtype=jnp.int32)
    common = jnp.bitwise_and(index[:, None], index[None, :])
    parity = jnp.zeros((order, order), jnp.int32)
    for level in range(max(order.bit_length() - 1, 0)):
        parity = parity + jnp.bitwise_and(jnp.right_shift(common, level), 1)
    return (1 - 2 * jnp.bitwise_and(parity, 1)).astype(jnp.float32)


def butterfly(vals):
    n = len(vals)
    half = 1
    while half < n:
        out = list(vals)
        for i in range(n):
            if not i & half:
                a, b = vals[i], vals[i | half]
                out[i] = a + b
                out[i | half] = a - b
        vals = out
        half *= 2
    return vals


def radix_pass(src, dst, rows, low, bits, post=None):
    span = 1 << bits
    stride = 1 << low
    for g in range(rows // span):
        base = (g // stride) * (stride * span) + g % stride
        vals = butterfly([src[base + j * stride] for j in range(span)])
        for j in range(span):
            dst[base + j * stride] = vals[j] if post is None else post(vals[j])


CHUNKS = 8


def split_rows(block):
    high = block.astype(jnp.bfloat16)
    rest = (block - high.astype(jnp.float32)).astype(jnp.bfloat16)
    return jnp.concatenate([high, rest], axis=0)


def pre_kernel(x_hbm, s_ref, h_ref, o_ref, buf, sems):
    blocks, chunks, cols, lanes = o_ref.shape
    copies = [
        pltpu.make_async_copy(x_hbm.at[:, i], buf.at[i], sems.at[i]) for i in range(chunks)
    ]
    for copy in copies:
        copy.start()
    low = 16
    for i, copy in enumerate(copies):
        copy.wait()
        block = buf[i]
        sign = s_ref[pl.ds(i, blocks, stride=chunks), :].astype(jnp.float32) * 2.0 - 1.0
        block = (block * sign[:, None, :]).reshape(blocks * cols, lanes)
        both = jnp.dot(split_rows(block), h_ref[...], preferred_element_type=jnp.float32)
        count = blocks * cols
        for g in range(blocks // low):
            vals = []
            for j in range(low):
                r = (g * low + j) * cols
                vals.append(both[r:r + cols] + both[count + r:count + r + cols])
            vals = butterfly(vals)
            for j in range(low):
                o_ref[g * low + j, i] = vals[j]
        for j in range(low):
            vals = butterfly([o_ref[g * low + j, i] for g in range(blocks // low)])
            for g in range(blocks // low):
                o_ref[g * low + j, i] = vals[g]


def pre_call(out_shape):
    blocks, chunks, cols, lanes = out_shape.shape
    return pl.pallas_call(
        pre_kernel,
        out_shape=out_shape,
        in_specs=[pl.BlockSpec(memory_space=pl.ANY)] + [pl.BlockSpec(memory_space=pltpu.VMEM)] * 2,
        out_specs=pl.BlockSpec(memory_space=pltpu.VMEM),
        scratch_shapes=[pltpu.VMEM((chunks, blocks, cols, lanes), jnp.float32),
                        pltpu.SemaphoreType.DMA((chunks,))],
        compiler_params=pltpu.CompilerParams(vmem_limit_bytes=24 * 1024 * 1024),
    )


def chunked_kernel(x_hbm, *refs, inner, outer, signed):
    if signed:
        s_ref, h_ref, o_ref, buf, sems = refs
    else:
        o_ref, buf, sems = refs
    rows = o_ref.shape[0]
    size = rows // CHUNKS
    copies = [
        pltpu.make_async_copy(x_hbm.at[pl.ds(i * size, size)], buf.at[pl.ds(i * size, size)], sems.at[i])
        for i in range(CHUNKS)
    ]
    for copy in copies:
        copy.start()

    for i, copy in enumerate(copies):
        copy.wait()
        rows_here = pl.ds(i * size, size)
        dst = o_ref.at[rows_here]
        if signed:
            block = buf[rows_here]
            sign = s_ref[rows_here, :].astype(jnp.float32) * 2.0 - 1.0
            block = (block * sign[:, None, :]).reshape(size * block.shape[1], block.shape[2])
            both = jnp.dot(split_rows(block), h_ref[...], preferred_element_type=jnp.float32)
            count = block.shape[0]
            dst[...] = (both[:count] + both[count:]).reshape(dst.shape)
            first = dst
        else:
            first = buf.at[rows_here]
        for n, (low, bits) in enumerate(inner):
            radix_pass(first if n == 0 else dst, dst, size, low, bits)
    for n, (low, bits, post) in enumerate(outer):
        radix_pass(o_ref, o_ref, rows, low, bits, post=post)


def chunked_call(out_shape, *, inner, outer, signed):
    n_vmem = 2 if signed else 0
    kernel = functools.partial(chunked_kernel, inner=inner, outer=outer, signed=signed)
    return pl.pallas_call(
        kernel,
        out_shape=out_shape,
        in_specs=[pl.BlockSpec(memory_space=pl.ANY)] + [pl.BlockSpec(memory_space=pltpu.VMEM)] * n_vmem,
        out_specs=pl.BlockSpec(memory_space=pltpu.VMEM),
        scratch_shapes=[pltpu.VMEM(out_shape.shape, jnp.float32), pltpu.SemaphoreType.DMA((CHUNKS,))],
        compiler_params=pltpu.CompilerParams(vmem_limit_bytes=24 * 1024 * 1024),
    )


def body(matrix_panel, sign_bits):
    columns, length = matrix_panel.shape
    devices = lax.axis_size("wide") * lax.axis_size("narrow")
    rows = length // LANES
    x = matrix_panel.reshape(columns, rows, LANES).transpose(1, 0, 2)
    signs = sign_bits.reshape(rows, LANES)
    shape = jax.ShapeDtypeStruct((rows, columns, LANES), jnp.float32)
    table = hadamard_table(LANES).astype(jnp.bfloat16)
    block_shape = jax.ShapeDtypeStruct((devices, rows // devices, columns, LANES), jnp.float32)
    blocks = pre_call(block_shape)(x.reshape(block_shape.shape), signs, table)
    gathered = lax.all_to_all(blocks, GROUP, 0, 0, tiled=True).reshape(rows, columns, LANES)
    scale = 1.0 / math.sqrt(length * devices)
    mid = chunked_call(shape, inner=((0, 4), (4, 3)), outer=((7, 3, lambda v: v * scale),), signed=False)
    mixed = mid(gathered)
    back = lax.all_to_all(mixed.reshape(blocks.shape), GROUP, 0, 0, tiled=True)
    return back.reshape(rows, columns, LANES).transpose(1, 0, 2).reshape(columns, length)


def solution(mesh):
    in_specs = (P(None, AXES), P(AXES))
    out_specs = P(None, AXES)
    return jax.shard_map(body, mesh=mesh, in_specs=in_specs, out_specs=out_specs, check_vma=False)
```

```python
import functools
import math

import jax
import jax.numpy as jnp
from jax import lax
from jax.experimental import pallas as pl
from jax.experimental.pallas import tpu as pltpu
from jax.sharding import PartitionSpec as P

AXES = ("wide", "narrow")
GROUP = ("narrow", "wide")
LANES = 128


def hadamard_table(order):
    index = jnp.arange(order, dtype=jnp.int32)
    common = jnp.bitwise_and(index[:, None], index[None, :])
    parity = jnp.zeros((order, order), jnp.int32)
    for level in range(max(order.bit_length() - 1, 0)):
        parity = parity + jnp.bitwise_and(jnp.right_shift(common, level), 1)
    return (1 - 2 * jnp.bitwise_and(parity, 1)).astype(jnp.float32)


def butterfly(vals):
    n = len(vals)
    half = 1
    while half < n:
        out = list(vals)
        for i in range(n):
            if not i & half:
                a, b = vals[i], vals[i | half]
                out[i] = a + b
                out[i | half] = a - b
        vals = out
        half *= 2
    return vals


def radix_pass(src, dst, rows, low, bits, post=None):
    span = 1 << bits
    stride = 1 << low
    for g in range(rows // span):
        base = (g // stride) * (stride * span) + g % stride
        vals = butterfly([src[base + j * stride] for j in range(span)])
        for j in range(span):
            dst[base + j * stride] = vals[j] if post is None else post(vals[j])


CHUNKS = 8


def split_rows(block):
    high = block.astype(jnp.bfloat16)
    rest = (block - high.astype(jnp.float32)).astype(jnp.bfloat16)
    return jnp.concatenate([high, rest], axis=0)


def pre_kernel(x_hbm, s_ref, h_ref, o_ref, buf, sems):
    blocks, chunks, cols, lanes = o_ref.shape
    copies = [
        pltpu.make_async_copy(x_hbm.at[:, i], buf.at[i], sems.at[i]) for i in range(chunks)
    ]
    for copy in copies:
        copy.start()
    low = 16
    for i, copy in enumerate(copies):
        copy.wait()
        block = buf[i]
        sign = s_ref[pl.ds(i, blocks, stride=chunks), :].astype(jnp.float32) * 2.0 - 1.0
        block = (block * sign[:, None, :]).reshape(blocks * cols, lanes)
        both = jnp.dot(split_rows(block), h_ref[...], preferred_element_type=jnp.float32)
        count = blocks * cols
        for g in range(blocks // low):
            vals = []
            for j in range(low):
                r = (g * low + j) * cols
                vals.append(both[r:r + cols] + both[count + r:count + r + cols])
            vals = butterfly(vals)
            for j in range(low):
                o_ref[g * low + j, i] = vals[j]
        for j in range(low):
            vals = butterfly([o_ref[g * low + j, i] for g in range(blocks // low)])
            for g in range(blocks // low):
                o_ref[g * low + j, i] = vals[g]


def pre_call(out_shape):
    blocks, chunks, cols, lanes = out_shape.shape
    return pl.pallas_call(
        pre_kernel,
        out_shape=out_shape,
        in_specs=[pl.BlockSpec(memory_space=pl.ANY)] + [pl.BlockSpec(memory_space=pltpu.VMEM)] * 2,
        out_specs=pl.BlockSpec(memory_space=pltpu.VMEM),
        scratch_shapes=[pltpu.VMEM((chunks, blocks, cols, lanes), jnp.float32),
                        pltpu.SemaphoreType.DMA((chunks,))],
        compiler_params=pltpu.CompilerParams(vmem_limit_bytes=48 * 1024 * 1024),
    )


def chunked_kernel(x_hbm, *refs, inner, outer, signed):
    if signed:
        s_ref, h_ref, o_ref, buf, sems = refs
    else:
        o_ref, buf, sems = refs
    rows = o_ref.shape[0]
    size = rows // CHUNKS
    copies = [
        pltpu.make_async_copy(x_hbm.at[pl.ds(i * size, size)], buf.at[pl.ds(i * size, size)], sems.at[i])
        for i in range(CHUNKS)
    ]
    for copy in copies:
        copy.start()

    for i, copy in enumerate(copies):
        copy.wait()
        rows_here = pl.ds(i * size, size)
        dst = o_ref.at[rows_here]
        if signed:
            block = buf[rows_here]
            sign = s_ref[rows_here, :].astype(jnp.float32) * 2.0 - 1.0
            block = (block * sign[:, None, :]).reshape(size * block.shape[1], block.shape[2])
            both = jnp.dot(split_rows(block), h_ref[...], preferred_element_type=jnp.float32)
            count = block.shape[0]
            dst[...] = (both[:count] + both[count:]).reshape(dst.shape)
            first = dst
        else:
            first = buf.at[rows_here]
        for n, (low, bits) in enumerate(inner):
            radix_pass(first if n == 0 else dst, dst, size, low, bits)
    for n, (low, bits, post) in enumerate(outer):
        radix_pass(o_ref, o_ref, rows, low, bits, post=post)


def chunked_call(out_shape, *, inner, outer, signed):
    n_vmem = 2 if signed else 0
    kernel = functools.partial(chunked_kernel, inner=inner, outer=outer, signed=signed)
    return pl.pallas_call(
        kernel,
        out_shape=out_shape,
        in_specs=[pl.BlockSpec(memory_space=pl.ANY)] + [pl.BlockSpec(memory_space=pltpu.VMEM)] * n_vmem,
        out_specs=pl.BlockSpec(memory_space=pltpu.VMEM),
        scratch_shapes=[pltpu.VMEM(out_shape.shape, jnp.float32), pltpu.SemaphoreType.DMA((CHUNKS,))],
        compiler_params=pltpu.CompilerParams(vmem_limit_bytes=16 * 1024 * 1024),
    )


def body(matrix_panel, sign_bits):
    columns, length = matrix_panel.shape
    devices = lax.axis_size("wide") * lax.axis_size("narrow")
    rows = length // LANES
    x = matrix_panel.reshape(columns, rows, LANES).transpose(1, 0, 2)
    signs = sign_bits.reshape(rows, LANES)
    shape = jax.ShapeDtypeStruct((rows, columns, LANES), jnp.float32)
    table = hadamard_table(LANES).astype(jnp.bfloat16)
    block_shape = jax.ShapeDtypeStruct((devices, rows // devices, columns, LANES), jnp.float32)
    blocks = pre_call(block_shape)(x.reshape(block_shape.shape), signs, table)
    gathered = lax.all_to_all(blocks, GROUP, 0, 0, tiled=True).reshape(rows, columns, LANES)
    scale = 1.0 / math.sqrt(length * devices)
    mid = chunked_call(shape, inner=((0, 4), (4, 3)), outer=((7, 3, lambda v: v * scale),), signed=False)
    mixed = mid(gathered)
    back = lax.all_to_all(mixed.reshape(blocks.shape), GROUP, 0, 0, tiled=True)
    return back.reshape(rows, columns, LANES).transpose(1, 0, 2).reshape(columns, length)


def solution(mesh):
    in_specs = (P(None, AXES), P(AXES))
    out_specs = P(None, AXES)
    return jax.shard_map(body, mesh=mesh, in_specs=in_specs, out_specs=out_specs, check_vma=False)
```

```python
import functools
import math

import jax
import jax.numpy as jnp
from jax import lax
from jax.experimental import pallas as pl
from jax.experimental.pallas import tpu as pltpu
from jax.sharding import PartitionSpec as P

AXES = ("wide", "narrow")
GROUP = ("narrow", "wide")
LANES = 128


def hadamard_table(order):
    index = jnp.arange(order, dtype=jnp.int32)
    common = jnp.bitwise_and(index[:, None], index[None, :])
    parity = jnp.zeros((order, order), jnp.int32)
    for level in range(max(order.bit_length() - 1, 0)):
        parity = parity + jnp.bitwise_and(jnp.right_shift(common, level), 1)
    return (1 - 2 * jnp.bitwise_and(parity, 1)).astype(jnp.float32)


def butterfly(vals):
    n = len(vals)
    half = 1
    while half < n:
        out = list(vals)
        for i in range(n):
            if not i & half:
                a, b = vals[i], vals[i | half]
                out[i] = a + b
                out[i | half] = a - b
        vals = out
        half *= 2
    return vals


def radix_pass(src, dst, rows, low, bits, post=None):
    span = 1 << bits
    stride = 1 << low
    for g in range(rows // span):
        base = (g // stride) * (stride * span) + g % stride
        vals = butterfly([src[base + j * stride] for j in range(span)])
        for j in range(span):
            dst[base + j * stride] = vals[j] if post is None else post(vals[j])


CHUNKS = 8


def split_rows(block):
    high = block.astype(jnp.bfloat16)
    rest = (block - high.astype(jnp.float32)).astype(jnp.bfloat16)
    return jnp.concatenate([high, rest], axis=0)


def pre_kernel(x_hbm, s_hbm, h_ref, o_hbm, buf, s_ref, obuf, sems, out_sems):
    blocks, chunks, cols, lanes = o_hbm.shape
    sign_copy = pltpu.make_async_copy(s_hbm, s_ref, sems.at[chunks])
    copies = [
        pltpu.make_async_copy(x_hbm.at[:, i], buf.at[i], sems.at[i]) for i in range(chunks)
    ]
    outs = [
        pltpu.make_async_copy(obuf.at[i], o_hbm.at[:, i], out_sems.at[i]) for i in range(chunks)
    ]
    sign_copy.start()
    for copy in copies:
        copy.start()
    sign_copy.wait()
    low = 16
    for i, copy in enumerate(copies):
        copy.wait()
        block = buf[i]
        sign = s_ref[pl.ds(i, blocks, stride=chunks), :].astype(jnp.float32) * 2.0 - 1.0
        block = (block * sign[:, None, :]).reshape(blocks * cols, lanes)
        both = jnp.dot(split_rows(block), h_ref[...], preferred_element_type=jnp.float32)
        count = blocks * cols
        dst = obuf.at[i]
        for g in range(blocks // low):
            vals = []
            for j in range(low):
                r = (g * low + j) * cols
                vals.append(both[r:r + cols] + both[count + r:count + r + cols])
            vals = butterfly(vals)
            for j in range(low):
                dst[g * low + j] = vals[j]
        for j in range(low):
            vals = butterfly([dst[g * low + j] for g in range(blocks // low)])
            for g in range(blocks // low):
                dst[g * low + j] = vals[g]
        outs[i].start()
    for out in outs:
        out.wait()


def pre_call(out_shape):
    blocks, chunks, cols, lanes = out_shape.shape
    return pl.pallas_call(
        pre_kernel,
        out_shape=out_shape,
        in_specs=[pl.BlockSpec(memory_space=pl.ANY)] * 2 + [pl.BlockSpec(memory_space=pltpu.VMEM)],
        out_specs=pl.BlockSpec(memory_space=pl.ANY),
        scratch_shapes=[pltpu.VMEM((chunks, blocks, cols, lanes), jnp.float32),
                        pltpu.VMEM((blocks * chunks, lanes), jnp.int32),
                        pltpu.VMEM((chunks, blocks, cols, lanes), jnp.float32),
                        pltpu.SemaphoreType.DMA((chunks + 1,)),
                        pltpu.SemaphoreType.DMA((chunks,))],
        compiler_params=pltpu.CompilerParams(vmem_limit_bytes=56 * 1024 * 1024),
    )


def chunked_kernel(x_hbm, *refs, inner, outer, signed):
    if signed:
        s_ref, h_ref, o_ref, buf, sems = refs
    else:
        o_ref, buf, sems = refs
    rows = o_ref.shape[0]
    size = rows // CHUNKS
    copies = [
        pltpu.make_async_copy(x_hbm.at[pl.ds(i * size, size)], buf.at[pl.ds(i * size, size)], sems.at[i])
        for i in range(CHUNKS)
    ]
    for copy in copies:
        copy.start()

    for i, copy in enumerate(copies):
        copy.wait()
        rows_here = pl.ds(i * size, size)
        dst = o_ref.at[rows_here]
        if signed:
            block = buf[rows_here]
            sign = s_ref[rows_here, :].astype(jnp.float32) * 2.0 - 1.0
            block = (block * sign[:, None, :]).reshape(size * block.shape[1], block.shape[2])
            both = jnp.dot(split_rows(block), h_ref[...], preferred_element_type=jnp.float32)
            count = block.shape[0]
            dst[...] = (both[:count] + both[count:]).reshape(dst.shape)
            first = dst
        else:
            first = buf.at[rows_here]
        for n, (low, bits) in enumerate(inner):
            radix_pass(first if n == 0 else dst, dst, size, low, bits)
    for n, (low, bits, post) in enumerate(outer):
        radix_pass(o_ref, o_ref, rows, low, bits, post=post)


def chunked_call(out_shape, *, inner, outer, signed):
    n_vmem = 2 if signed else 0
    kernel = functools.partial(chunked_kernel, inner=inner, outer=outer, signed=signed)
    return pl.pallas_call(
        kernel,
        out_shape=out_shape,
        in_specs=[pl.BlockSpec(memory_space=pl.ANY)] + [pl.BlockSpec(memory_space=pltpu.VMEM)] * n_vmem,
        out_specs=pl.BlockSpec(memory_space=pltpu.VMEM),
        scratch_shapes=[pltpu.VMEM(out_shape.shape, jnp.float32), pltpu.SemaphoreType.DMA((CHUNKS,))],
        compiler_params=pltpu.CompilerParams(vmem_limit_bytes=16 * 1024 * 1024),
    )


def body(matrix_panel, sign_bits):
    columns, length = matrix_panel.shape
    devices = lax.axis_size("wide") * lax.axis_size("narrow")
    rows = length // LANES
    x = matrix_panel.reshape(columns, rows, LANES).transpose(1, 0, 2)
    signs = sign_bits.reshape(rows, LANES)
    shape = jax.ShapeDtypeStruct((rows, columns, LANES), jnp.float32)
    table = hadamard_table(LANES).astype(jnp.bfloat16)
    block_shape = jax.ShapeDtypeStruct((devices, rows // devices, columns, LANES), jnp.float32)
    blocks = pre_call(block_shape)(x.reshape(block_shape.shape), signs, table)
    gathered = lax.all_to_all(blocks, GROUP, 0, 0, tiled=True).reshape(rows, columns, LANES)
    scale = 1.0 / math.sqrt(length * devices)
    mid = chunked_call(shape, inner=((0, 4), (4, 3)), outer=((7, 3, lambda v: v * scale),), signed=False)
    mixed = mid(gathered)
    back = lax.all_to_all(mixed.reshape(blocks.shape), GROUP, 0, 0, tiled=True)
    return back.reshape(rows, columns, LANES).transpose(1, 0, 2).reshape(columns, length)


def solution(mesh):
    in_specs = (P(None, AXES), P(AXES))
    out_specs = P(None, AXES)
    return jax.shard_map(body, mesh=mesh, in_specs=in_specs, out_specs=out_specs, check_vma=False)
```

```python
import functools
import math

import jax
import jax.numpy as jnp
from jax import lax
from jax.experimental import pallas as pl
from jax.experimental.pallas import tpu as pltpu
from jax.sharding import PartitionSpec as P

AXES = ("wide", "narrow")
GROUP = ("narrow", "wide")
LANES = 128
LIFT_BITS = 64
LIFT = float(2.0 ** LIFT_BITS)


def hadamard_table(order):
    index = jnp.arange(order, dtype=jnp.int32)
    common = jnp.bitwise_and(index[:, None], index[None, :])
    parity = jnp.zeros((order, order), jnp.int32)
    for level in range(max(order.bit_length() - 1, 0)):
        parity = parity + jnp.bitwise_and(jnp.right_shift(common, level), 1)
    return (1 - 2 * jnp.bitwise_and(parity, 1)).astype(jnp.float32)


def butterfly(vals):
    n = len(vals)
    half = 1
    while half < n:
        out = list(vals)
        for i in range(n):
            if not i & half:
                a, b = vals[i], vals[i | half]
                out[i] = a + b
                out[i | half] = a - b
        vals = out
        half *= 2
    return vals


def radix_pass(src, dst, rows, low, bits, post=None):
    span = 1 << bits
    stride = 1 << low
    for g in range(rows // span):
        base = (g // stride) * (stride * span) + g % stride
        vals = butterfly([src[base + j * stride] for j in range(span)])
        for j in range(span):
            dst[base + j * stride] = vals[j] if post is None else post(vals[j])


CHUNKS = 8


def split_rows(block):
    high = block.astype(jnp.bfloat16)
    rest = (block - high.astype(jnp.float32)).astype(jnp.bfloat16)
    return jnp.concatenate([high, rest], axis=0)


def pre_kernel(x_hbm, s_ref, h_ref, o_ref, buf, sems):
    blocks, chunks, cols, lanes = o_ref.shape
    copies = [
        pltpu.make_async_copy(x_hbm.at[:, i], buf.at[i], sems.at[i]) for i in range(chunks)
    ]
    for copy in copies:
        copy.start()
    low = 16
    for i, copy in enumerate(copies):
        copy.wait()
        block = buf[i]
        sign = (s_ref[pl.ds(i, blocks, stride=chunks), :].astype(jnp.float32) * 2.0 - 1.0) * LIFT
        block = (block * sign[:, None, :]).reshape(blocks * cols, lanes)
        both = jnp.dot(split_rows(block), h_ref[...], preferred_element_type=jnp.float32)
        count = blocks * cols
        for g in range(blocks // low):
            vals = []
            for j in range(low):
                r = (g * low + j) * cols
                vals.append(both[r:r + cols] + both[count + r:count + r + cols])
            vals = butterfly(vals)
            for j in range(low):
                o_ref[g * low + j, i] = vals[j]
        for j in range(low):
            vals = butterfly([o_ref[g * low + j, i] for g in range(blocks // low)])
            for g in range(blocks // low):
                o_ref[g * low + j, i] = vals[g]


def pre_call(out_shape):
    blocks, chunks, cols, lanes = out_shape.shape
    return pl.pallas_call(
        pre_kernel,
        out_shape=out_shape,
        in_specs=[pl.BlockSpec(memory_space=pl.ANY)] + [pl.BlockSpec(memory_space=pltpu.VMEM)] * 2,
        out_specs=pl.BlockSpec(memory_space=pltpu.VMEM),
        scratch_shapes=[pltpu.VMEM((chunks, blocks, cols, lanes), jnp.float32),
                        pltpu.SemaphoreType.DMA((chunks,))],
        compiler_params=pltpu.CompilerParams(vmem_limit_bytes=48 * 1024 * 1024),
    )


def chunked_kernel(x_hbm, *refs, inner, outer, signed):
    if signed:
        s_ref, h_ref, o_ref, buf, sems = refs
    else:
        o_ref, buf, sems = refs
    rows = o_ref.shape[0]
    size = rows // CHUNKS
    copies = [
        pltpu.make_async_copy(x_hbm.at[pl.ds(i * size, size)], buf.at[pl.ds(i * size, size)], sems.at[i])
        for i in range(CHUNKS)
    ]
    for copy in copies:
        copy.start()

    for i, copy in enumerate(copies):
        copy.wait()
        rows_here = pl.ds(i * size, size)
        dst = o_ref.at[rows_here]
        if signed:
            block = buf[rows_here]
            sign = s_ref[rows_here, :].astype(jnp.float32) * 2.0 - 1.0
            block = (block * sign[:, None, :]).reshape(size * block.shape[1], block.shape[2])
            both = jnp.dot(split_rows(block), h_ref[...], preferred_element_type=jnp.float32)
            count = block.shape[0]
            dst[...] = (both[:count] + both[count:]).reshape(dst.shape)
            first = dst
        else:
            first = buf.at[rows_here]
        for n, (low, bits) in enumerate(inner):
            radix_pass(first if n == 0 else dst, dst, size, low, bits)
    for n, (low, bits, post) in enumerate(outer):
        radix_pass(o_ref, o_ref, rows, low, bits, post=post)


def chunked_call(out_shape, *, inner, outer, signed):
    n_vmem = 2 if signed else 0
    kernel = functools.partial(chunked_kernel, inner=inner, outer=outer, signed=signed)
    return pl.pallas_call(
        kernel,
        out_shape=out_shape,
        in_specs=[pl.BlockSpec(memory_space=pl.ANY)] + [pl.BlockSpec(memory_space=pltpu.VMEM)] * n_vmem,
        out_specs=pl.BlockSpec(memory_space=pltpu.VMEM),
        scratch_shapes=[pltpu.VMEM(out_shape.shape, jnp.float32), pltpu.SemaphoreType.DMA((CHUNKS,))],
        compiler_params=pltpu.CompilerParams(vmem_limit_bytes=16 * 1024 * 1024),
    )


def body(matrix_panel, sign_bits):
    columns, length = matrix_panel.shape
    devices = lax.axis_size("wide") * lax.axis_size("narrow")
    rows = length // LANES
    x = matrix_panel.reshape(columns, rows, LANES).transpose(1, 0, 2)
    signs = sign_bits.reshape(rows, LANES)
    shape = jax.ShapeDtypeStruct((rows, columns, LANES), jnp.float32)
    table = hadamard_table(LANES).astype(jnp.bfloat16)
    block_shape = jax.ShapeDtypeStruct((devices, rows // devices, columns, LANES), jnp.float32)
    blocks = pre_call(block_shape)(x.reshape(block_shape.shape), signs, table)
    gathered = lax.all_to_all(blocks, GROUP, 0, 0, tiled=True).reshape(rows, columns, LANES)
    scale = 2.0 ** -LIFT_BITS / math.sqrt(length * devices)
    mid = chunked_call(shape, inner=((0, 4), (4, 3)), outer=((7, 3, lambda v: v * scale),), signed=False)
    mixed = mid(gathered)
    back = lax.all_to_all(mixed.reshape(blocks.shape), GROUP, 0, 0, tiled=True)
    return back.reshape(rows, columns, LANES).transpose(1, 0, 2).reshape(columns, length)


def solution(mesh):
    in_specs = (P(None, AXES), P(AXES))
    out_specs = P(None, AXES)
    return jax.shard_map(body, mesh=mesh, in_specs=in_specs, out_specs=out_specs, check_vma=False)
```
